256 devices in a mesh: ctx: 32 (over y_lo, z, core), tp: 8 (over y_hi, x).
Axes of the slice: x: 4, y: 4 (y_hi: 2, y_lo: 2; y = y_hi * 2 + y_lo), z: 8, core: 2. Of those that a mesh axis runs over, the one named last changes fastest.
Arguments:
- queries: bfloat16 [4096, 8192], P('ctx', 'tp'), may hold values from -32 to 32
- key_proj: bfloat16 [4096, 1024], P('ctx', 'tp'), may hold values from -12.5 to 12.5
- value_proj: bfloat16 [4096, 1024], P('ctx', 'tp'), may hold values from -6 to 6
- grad_out: bfloat16 [4096, 8192], P('ctx', 'tp'), may hold values from -6 to 6
- key_weight: bfloat16 [8192, 1024], P(None, 'tp'), may hold values from -0.1875 to 0.1875
- value_weight: bfloat16 [8192, 1024], P(None, 'tp'), may hold values from -0.1875 to 0.1875
- doc_start: int32 [4096], P('ctx'), may hold values from 0 to 4095, as said below
Outputs:
- grad_query: bfloat16 [4096, 8192], P('ctx', 'tp')
- grad_key: bfloat16 [4096, 1024], P('ctx', 'tp')
- grad_value: bfloat16 [4096, 1024], P('ctx', 'tp')
- grad_input: bfloat16 [4096, 8192], P('ctx', 'tp')
The draws below stay inside these ranges and needn't reach their ends.
Inputs may be any that keep to these rules, and one draw needn't show every extreme that they name: doc_start[p] is the first position of the document holding p; documents are runs of consecutive positions, each of 1 to 2048 positions; the first document has exactly 2048 positions and the last position is a document of its own.
All inputs are finite; a program needn't handle non-finite values.
Results may differ from the reference program's by a relative error of at most 0.034.
Values may be sent and summed in bfloat16 or wider, within the bound.
No kernel may reach another device: no remote copies, remote signals or barrier semaphores. Data moves between devices by JAX's collectives and lax.ppermute only.
A program may use at most 64 MiB of HBM per device.

```python
import math
import jax
import jax.numpy as jnp
from jax import lax

D = 8192
HEADS = 64
KV_HEADS = 8
HD = 128
TOK_DEV = 128
DOC_MOST = 2048
TOKENS = 4096
REACH = 16


def shared_keys(key):
    base_keys = jax.random.normal(jax.random.fold_in(key, 11), (TOKENS, KV_HEADS * HD), jnp.float32)
    base_keys = jnp.clip(base_keys, -4.0, 4.0)
    return base_keys


def draw_key_proj(key, part):
    return shared_keys(key).astype(jnp.bfloat16)


def draw_queries(key, part):
    drawn = jnp.clip(jax.random.normal(jax.random.fold_in(key, 23), (TOKENS, HEADS * HD), jnp.float32), -4.0, 4.0)
    return drawn.astype(jnp.bfloat16)


def draw_doc_start(key, part):
    lengths = jax.random.randint(jax.random.fold_in(key, 5), (TOKENS,), 1, DOC_MOST + 1)
    lengths = jnp.where(jnp.arange(TOKENS) == 0, DOC_MOST, lengths).astype(jnp.int32)
    ends = jnp.cumsum(lengths).astype(jnp.int32)
    starts = ends - lengths
    positions = jnp.arange(TOKENS, dtype=jnp.int32)
    doc_index = jnp.searchsorted(ends, positions, side='right')
    first = starts[doc_index].astype(jnp.int32)
    return jnp.where(positions == TOKENS - 1, TOKENS - 1, first).astype(jnp.int32)


def levels(rng, dims, split, smallest, top_value):
    loudness, own = 1.0, jax.random.fold_in(rng, 6)
    for position, shards_of in split:
        heights = jnp.exp(jax.random.uniform(jax.random.fold_in(own, position), (shards_of,), jnp.float32, smallest / len(split), top_value / len(split)))
        loudness = loudness * jnp.repeat(heights, dims[position] // shards_of).reshape([-1 if axis == position else 1 for axis in range(len(dims))])
    return loudness


def normal_values(key, extent, spread, most, cuts=(), kind=jnp.bfloat16):
    values = jax.random.normal(key, extent, jnp.float32) * spread
    if len(cuts) > 0:
        values = levels(key, extent, cuts, -0.22, 0.18) * values
    return jnp.clip(values, min=-most, max=most).astype(kind)


def setup_inputs(seed: int = 0) -> dict:
    keys = jax.random.split(jax.random.key(seed), 8)
    queries = draw_queries(jax.random.fold_in(keys[7], 71), 0)
    key_proj = draw_key_proj(jax.random.fold_in(keys[7], 71), 0)
    value_proj = normal_values(keys[2], (TOKENS, KV_HEADS * HD), 1.0, 6.0, ((0, 32), (1, 8)))
    grad_out = normal_values(keys[3], (TOKENS, HEADS * HD), 1.0, 6.0, ((0, 32), (1, 8)))
    key_weight = normal_values(keys[4], (D, KV_HEADS * HD), (KV_HEADS * HD) ** -0.5, 0.1875, ((1, 8),))
    value_weight = normal_values(keys[5], (D, KV_HEADS * HD), (KV_HEADS * HD) ** -0.5, 0.1875, ((1, 8),))
    doc_start = draw_doc_start(jax.random.fold_in(keys[7], 71), 0)
    return {"queries": queries, "key_proj": key_proj, "value_proj": value_proj, "grad_out": grad_out, "key_weight": key_weight, "value_weight": value_weight, "doc_start": doc_start}


def rounded(values):
    return lax.optimization_barrier(values.astype(jnp.bfloat16)).astype(jnp.float32)

def reference(queries, key_proj, value_proj, grad_out, key_weight, value_weight, doc_start):
    group_size = HEADS // KV_HEADS
    soft_scale = 1.0 / math.sqrt(HD)
    window = (REACH + 1) * TOK_DEV
    blocks = TOKENS // TOK_DEV

    def one_block(loop_carry, blk_index):
        grad_keys, grad_values = loop_carry
        query_start = (blk_index * TOK_DEV).astype(jnp.int32)
        key_start = (jnp.maximum(blk_index - REACH, 0) * TOK_DEV).astype(jnp.int32)
        query_rows = lax.dynamic_slice_in_dim(queries, query_start, TOK_DEV, 0).astype(jnp.float32)
        query_rows = query_rows.reshape(TOK_DEV, KV_HEADS, group_size, HD)
        cot_rows = lax.dynamic_slice_in_dim(grad_out, query_start, TOK_DEV, 0).astype(jnp.float32)
        cot_rows = cot_rows.reshape(TOK_DEV, KV_HEADS, group_size, HD)
        key_rows = lax.dynamic_slice_in_dim(key_proj, key_start, window, 0).astype(jnp.float32).reshape(window, KV_HEADS, HD)
        value_rows = lax.dynamic_slice_in_dim(value_proj, key_start, window, 0).astype(jnp.float32).reshape(window, KV_HEADS, HD)
        query_pos = query_start + jnp.arange(TOK_DEV, dtype=jnp.int32)
        key_pos = key_start + jnp.arange(window, dtype=jnp.int32)
        first_pos = lax.dynamic_slice_in_dim(doc_start, query_start, TOK_DEV, 0)
        visible = (key_pos[None, :] <= query_pos[:, None]) & (key_pos[None, :] >= first_pos[:, None])
        scores = jnp.einsum('qkgd,pkd->kgqp', query_rows, key_rows) * soft_scale
        scores = jnp.where(visible, scores, -jnp.inf)
        rowmax = lax.optimization_barrier(jnp.max(scores, axis=-1, keepdims=True))
        expw = jnp.exp(scores - rowmax)
        row_total = lax.optimization_barrier(jnp.sum(expw, axis=-1, keepdims=True))
        attn_out = jnp.einsum('kgqp,pkd->kgqd', rounded(expw), value_rows) / row_total
        attn_out = rounded(attn_out)
        log_total = rowmax + jnp.log(row_total)
        delta = jnp.einsum('qkgd,kgqd->kgq', cot_rows, attn_out)[..., None]
        probs = jnp.exp(scores - log_total)
        grad_probs = jnp.einsum('qkgd,pkd->kgqp', cot_rows, value_rows)
        grad_scores = rounded(probs * (grad_probs - delta))
        grad_q = jnp.einsum('kgqp,pkd->qkgd', grad_scores, key_rows) * soft_scale
        key_part = jnp.einsum('kgqp,qkgd->pkd', grad_scores, query_rows) * soft_scale
        value_part = jnp.einsum('kgqp,qkgd->pkd', rounded(probs), cot_rows)
        old_keys = lax.dynamic_slice_in_dim(grad_keys, key_start, window, 0)
        old_values = lax.dynamic_slice_in_dim(grad_values, key_start, window, 0)
        grad_keys = lax.dynamic_update_slice_in_dim(grad_keys, old_keys + key_part.reshape(window, KV_HEADS * HD), key_start, 0)
        grad_values = lax.dynamic_update_slice_in_dim(grad_values, old_values + value_part.reshape(window, KV_HEADS * HD), key_start, 0)
        return ((grad_keys, grad_values), grad_q.reshape(TOK_DEV, HEADS * HD).astype(jnp.bfloat16))
    zeros_kv = jnp.zeros((TOKENS, KV_HEADS * HD), jnp.float32)
    (grad_keys, grad_values), grad_blocks = lax.scan(one_block, (zeros_kv, zeros_kv), jnp.arange(blocks, dtype=jnp.int32))
    grad_query = grad_blocks.reshape(TOKENS, HEADS * HD)
    grad_key = grad_keys.astype(jnp.bfloat16)
    grad_value = grad_values.astype(jnp.bfloat16)
    grad_input = jnp.einsum('tc,dc->td', grad_key.astype(jnp.float32), key_weight.astype(jnp.float32))
    grad_input = grad_input + jnp.einsum('tc,dc->td', grad_value.astype(jnp.float32), value_weight.astype(jnp.float32))
    return (grad_query, grad_key, grad_value, grad_input.astype(jnp.bfloat16))
```

```python
import math

import jax
import jax.numpy as jnp
from jax import lax
from jax.sharding import PartitionSpec as P

HEADS = 64
KV_HEADS = 8
HD = 128
REACH = 16


NEGATIVE = -1e30


def shifted(value, axis, steps):
    count = lax.axis_size(axis)
    pairs = [(source, source + steps) for source in range(count) if 0 <= source + steps < count]
    return lax.ppermute(value, axis, pairs)


def shards(queries, key_proj, value_proj, grad_out, key_weight, value_weight, doc_start):
    tok_rows = queries.shape[0]
    heads_kv = key_proj.shape[1] // HD
    kv_cols = key_proj.shape[1]
    group_size = HEADS // KV_HEADS
    soft_scale = 1.0 / math.sqrt(HD)
    my_index = lax.axis_index("ctx")
    blocks = REACH + 1
    window = blocks * tok_rows

    own_kv = jnp.concatenate([key_proj, value_proj], axis=1)
    half = REACH // 2
    same_core = [shifted(own_kv, "ctx", 2 * (i + 1)) for i in range(half)]
    stack = jnp.concatenate([own_kv] + same_core, axis=0)
    parity = my_index % 2
    sibling = [(source, source ^ 1) for source in range(lax.axis_size("ctx"))]
    outgoing = lax.dynamic_slice_in_dim(stack, parity * tok_rows, half * tok_rows, 0)
    other_core = lax.ppermute(outgoing, "ctx", sibling)
    window_kv = jnp.concatenate([stack[tok_rows:], other_core, own_kv], axis=0)
    offsets = [2 * (i + 1) for i in range(half)] + [2 * i + 1 for i in range(half)] + [0]
    keys_three = window_kv[:, :kv_cols].reshape(window, heads_kv, HD)
    values_three = window_kv[:, kv_cols:].reshape(window, heads_kv, HD)

    query_four = queries.reshape(tok_rows, heads_kv, group_size, HD)
    grad_four = grad_out.reshape(tok_rows, heads_kv, group_size, HD)
    query_pos = my_index * tok_rows + jnp.arange(tok_rows, dtype=jnp.int32)
    block_pos = jnp.concatenate(
        [jnp.full((tok_rows,), offset, jnp.int32) for offset in offsets]
    )
    key_pos = (my_index * tok_rows - block_pos * tok_rows) + jnp.tile(
        jnp.arange(tok_rows, dtype=jnp.int32), blocks
    )
    visible = (key_pos[None, :] <= query_pos[:, None]) & (key_pos[None, :] >= doc_start[:, None])

    scores = (
        jnp.einsum("qkgd,pkd->kgqp", query_four, keys_three, preferred_element_type=jnp.float32)
        * soft_scale
    )
    scores = jnp.where(visible, scores, NEGATIVE)
    rowmax = jnp.max(scores, axis=-1)
    expw = jnp.exp(scores - rowmax[..., None])
    row_total = jnp.sum(expw, axis=-1)
    acc_sum = jnp.einsum(
        "kgqp,pkd->kgqd",
        expw.astype(jnp.bfloat16),
        values_three,
        preferred_element_type=jnp.float32,
    )
    attn_out = (acc_sum / row_total[..., None]).astype(jnp.bfloat16)
    log_total = rowmax + jnp.log(row_total)
    delta = jnp.einsum("qkgd,kgqd->kgq", grad_four, attn_out, preferred_element_type=jnp.float32)

    probs = jnp.exp(scores - log_total[..., None])
    value_part = jnp.einsum(
        "kgqp,qkgd->pkd", probs.astype(jnp.bfloat16), grad_four, preferred_element_type=jnp.float32
    )
    grad_probs = jnp.einsum(
        "qkgd,pkd->kgqp", grad_four, values_three, preferred_element_type=jnp.float32
    )
    grad_scores = (probs * (grad_probs - delta[..., None])).astype(jnp.bfloat16)
    query_part = (
        jnp.einsum("kgqp,pkd->qkgd", grad_scores, keys_three, preferred_element_type=jnp.float32)
        * soft_scale
    )
    key_part = (
        jnp.einsum("kgqp,qkgd->pkd", grad_scores, query_four, preferred_element_type=jnp.float32)
        * soft_scale
    )
    grad_query = query_part.reshape(tok_rows, heads_kv * group_size * HD).astype(jnp.bfloat16)

    partial_kv = jnp.concatenate(
        [key_part.reshape(window, kv_cols), value_part.reshape(window, kv_cols)], axis=1
    )
    span = half * tok_rows
    from_other = lax.ppermute(partial_kv[span : 2 * span].astype(jnp.bfloat16), "ctx", sibling)
    back_stack = jnp.concatenate([partial_kv[2 * span :], partial_kv[:span]], axis=0)
    back_stack = lax.dynamic_update_slice_in_dim(
        back_stack,
        lax.dynamic_slice_in_dim(back_stack, parity * tok_rows, span, 0)
        + from_other.astype(jnp.float32),
        parity * tok_rows,
        0,
    )
    total_kv = back_stack[:tok_rows]
    for i in range(half):
        piece = back_stack[(i + 1) * tok_rows : (i + 2) * tok_rows].astype(jnp.bfloat16)
        total_kv = total_kv + shifted(piece, "ctx", -2 * (i + 1)).astype(jnp.float32)
    grad_key = total_kv[:, :kv_cols].astype(jnp.bfloat16)
    grad_value = total_kv[:, kv_cols:].astype(jnp.bfloat16)

    partial_input = jnp.einsum(
        "rc,dc->rd", grad_key, key_weight, preferred_element_type=jnp.float32
    )
    partial_input = partial_input + jnp.einsum(
        "rc,dc->rd", grad_value, value_weight, preferred_element_type=jnp.float32
    )
    tp_size = lax.axis_size("tp")
    tp_index = lax.axis_index("tp")
    chunks = partial_input.astype(jnp.bfloat16).reshape(tok_rows, tp_size, -1)
    total_input = jnp.take(chunks, tp_index, axis=1).astype(jnp.float32)
    for k in range(1, tp_size):
        piece = jnp.take(chunks, (tp_index + k) % tp_size, axis=1)
        pairs = [(source, (source + k) % tp_size) for source in range(tp_size)]
        total_input = total_input + lax.ppermute(piece, "tp", pairs).astype(jnp.float32)
    grad_input = total_input.astype(jnp.bfloat16)
    return (grad_query, grad_key, grad_value, grad_input)


def solution(mesh):
    in_specs = (
        P("ctx", "tp"),
        P("ctx", "tp"),
        P("ctx", "tp"),
        P("ctx", "tp"),
        P(None, "tp"),
        P(None, "tp"),
        P("ctx"),
    )
    out_specs = (P("ctx", "tp"), P("ctx", "tp"), P("ctx", "tp"), P("ctx", "tp"))
    return jax.shard_map(shards, mesh=mesh, in_specs=in_specs, out_specs=out_specs, check_vma=False)
```

```python
import math

import jax
import jax.numpy as jnp
from jax import lax
from jax.sharding import PartitionSpec as P

HEADS = 64
KV_HEADS = 8
HD = 128
REACH = 16


NEGATIVE = -1e30


def shifted(value, axis, steps):
    count = lax.axis_size(axis)
    pairs = [(source, source + steps) for source in range(count) if 0 <= source + steps < count]
    return lax.ppermute(value, axis, pairs)


def shards(queries, key_proj, value_proj, grad_out, key_weight, value_weight, doc_start):
    tok_rows = queries.shape[0]
    heads_kv = key_proj.shape[1] // HD
    kv_cols = key_proj.shape[1]
    group_size = HEADS // KV_HEADS
    soft_scale = 1.0 / math.sqrt(HD)
    my_index = lax.axis_index("ctx")
    blocks = REACH + 1
    window = blocks * tok_rows

    tp_size = lax.axis_size("tp")
    tp_index = lax.axis_index("tp")
    both_weights = jnp.concatenate([key_weight, value_weight], axis=1)
    d_rows = both_weights.shape[0] // tp_size
    weight_rows = both_weights.reshape(tp_size, d_rows, 2 * kv_cols)
    own_rows = jnp.take(weight_rows, tp_index, axis=0)
    weight_pieces = [None]
    for k in range(1, tp_size):
        pairs = [(source, (source + k) % tp_size) for source in range(tp_size)]
        piece = jnp.take(weight_rows, (tp_index + k) % tp_size, axis=0)
        weight_pieces.append(lax.ppermute(piece, "tp", pairs))

    own_kv = jnp.concatenate([key_proj, value_proj], axis=1)
    half = REACH // 2
    same_core = [shifted(own_kv, "ctx", 2 * (i + 1)) for i in range(half)]
    stack = jnp.concatenate([own_kv] + same_core, axis=0)
    parity = my_index % 2
    sibling = [(source, source ^ 1) for source in range(lax.axis_size("ctx"))]
    outgoing = lax.dynamic_slice_in_dim(stack, parity * tok_rows, half * tok_rows, 0)
    other_core = lax.ppermute(outgoing, "ctx", sibling)
    window_kv = jnp.concatenate([stack[tok_rows:], other_core, own_kv], axis=0)
    offsets = [2 * (i + 1) for i in range(half)] + [2 * i + 1 for i in range(half)] + [0]
    keys_three = window_kv[:, :kv_cols].reshape(window, heads_kv, HD)
    values_three = window_kv[:, kv_cols:].reshape(window, heads_kv, HD)

    query_four = queries.reshape(tok_rows, heads_kv, group_size, HD)
    grad_four = grad_out.reshape(tok_rows, heads_kv, group_size, HD)
    query_pos = my_index * tok_rows + jnp.arange(tok_rows, dtype=jnp.int32)
    block_pos = jnp.concatenate(
        [jnp.full((tok_rows,), offset, jnp.int32) for offset in offsets]
    )
    key_pos = (my_index * tok_rows - block_pos * tok_rows) + jnp.tile(
        jnp.arange(tok_rows, dtype=jnp.int32), blocks
    )
    visible = (key_pos[None, :] <= query_pos[:, None]) & (key_pos[None, :] >= doc_start[:, None])

    scores = (
        jnp.einsum("qkgd,pkd->kgqp", query_four, keys_three, preferred_element_type=jnp.float32)
        * soft_scale
    )
    scores = jnp.where(visible, scores, NEGATIVE)
    rowmax = jnp.max(scores, axis=-1)
    expw = jnp.exp(scores - rowmax[..., None])
    row_total = jnp.sum(expw, axis=-1)
    acc_sum = jnp.einsum(
        "kgqp,pkd->kgqd",
        expw.astype(jnp.bfloat16),
        values_three,
        preferred_element_type=jnp.float32,
    )
    attn_out = (acc_sum / row_total[..., None]).astype(jnp.bfloat16)
    log_total = rowmax + jnp.log(row_total)
    delta = jnp.einsum("qkgd,kgqd->kgq", grad_four, attn_out, preferred_element_type=jnp.float32)

    probs = jnp.exp(scores - log_total[..., None])
    value_part = jnp.einsum(
        "kgqp,qkgd->pkd", probs.astype(jnp.bfloat16), grad_four, preferred_element_type=jnp.float32
    )
    grad_probs = jnp.einsum(
        "qkgd,pkd->kgqp", grad_four, values_three, preferred_element_type=jnp.float32
    )
    grad_scores = (probs * (grad_probs - delta[..., None])).astype(jnp.bfloat16)
    query_part = (
        jnp.einsum("kgqp,pkd->qkgd", grad_scores, keys_three, preferred_element_type=jnp.float32)
        * soft_scale
    )
    key_part = (
        jnp.einsum("kgqp,qkgd->pkd", grad_scores, query_four, preferred_element_type=jnp.float32)
        * soft_scale
    )
    grad_query = query_part.reshape(tok_rows, heads_kv * group_size * HD).astype(jnp.bfloat16)

    partial_kv = jnp.concatenate(
        [key_part.reshape(window, kv_cols), value_part.reshape(window, kv_cols)], axis=1
    )
    span = half * tok_rows
    from_other = lax.ppermute(partial_kv[span : 2 * span].astype(jnp.bfloat16), "ctx", sibling)
    back_stack = jnp.concatenate([partial_kv[2 * span :], partial_kv[:span]], axis=0)
    back_stack = lax.dynamic_update_slice_in_dim(
        back_stack,
        lax.dynamic_slice_in_dim(back_stack, parity * tok_rows, span, 0)
        + from_other.astype(jnp.float32),
        parity * tok_rows,
        0,
    )
    total_kv = back_stack[:tok_rows]
    for i in range(half):
        piece = back_stack[(i + 1) * tok_rows : (i + 2) * tok_rows].astype(jnp.bfloat16)
        total_kv = total_kv + shifted(piece, "ctx", -2 * (i + 1)).astype(jnp.float32)
    grad_key = total_kv[:, :kv_cols].astype(jnp.bfloat16)
    grad_value = total_kv[:, kv_cols:].astype(jnp.bfloat16)
    own_grads = jnp.concatenate([grad_key, grad_value], axis=1)
    late_pieces, own_grads = lax.optimization_barrier((weight_pieces[1:], own_grads))

    gathered_grads = [own_grads]
    gathered_weights = [own_rows]
    for k in range(1, tp_size):
        pairs = [(source, (source + k) % tp_size) for source in range(tp_size)]
        gathered_grads.append(lax.ppermute(own_grads, "tp", pairs))
        gathered_weights.append(late_pieces[k - 1])
    grads_all = jnp.concatenate(gathered_grads, axis=1)
    weights_all = jnp.concatenate(gathered_weights, axis=1)
    grad_input = jnp.einsum(
        "rc,dc->rd", grads_all, weights_all, preferred_element_type=jnp.float32
    ).astype(jnp.bfloat16)
    return (grad_query, grad_key, grad_value, grad_input)


def solution(mesh):
    in_specs = (
        P("ctx", "tp"),
        P("ctx", "tp"),
        P("ctx", "tp"),
        P("ctx", "tp"),
        P(None, "tp"),
        P(None, "tp"),
        P("ctx"),
    )
    out_specs = (P("ctx", "tp"), P("ctx", "tp"), P("ctx", "tp"), P("ctx", "tp"))
    return jax.shard_map(shards, mesh=mesh, in_specs=in_specs, out_specs=out_specs, check_vma=False)
```

```python
import math

import jax
import jax.numpy as jnp
from jax import lax
from jax.sharding import PartitionSpec as P

HEADS = 64
KV_HEADS = 8
HD = 128
REACH = 16


NEGATIVE = -1e30


def shifted(value, axis, steps):
    count = lax.axis_size(axis)
    pairs = [(source, source + steps) for source in range(count) if 0 <= source + steps < count]
    return lax.ppermute(value, axis, pairs)


def shards(queries, key_proj, value_proj, grad_out, key_weight, value_weight, doc_start):
    tok_rows = queries.shape[0]
    heads_kv = key_proj.shape[1] // HD
    kv_cols = key_proj.shape[1]
    group_size = HEADS // KV_HEADS
    soft_scale = 1.0 / math.sqrt(HD)
    my_index = lax.axis_index("ctx")
    blocks = REACH + 1
    window = blocks * tok_rows

    tp_size = lax.axis_size("tp")
    tp_index = lax.axis_index("tp")
    d_rows = key_weight.shape[0] // tp_size

    def weight_piece(target):
        return jnp.concatenate(
            [
                lax.dynamic_slice_in_dim(key_weight, target * d_rows, d_rows, 0),
                lax.dynamic_slice_in_dim(value_weight, target * d_rows, d_rows, 0),
            ],
            axis=1,
        )

    own_rows = weight_piece(tp_index)
    weight_pieces = [None]
    for k in range(1, tp_size):
        pairs = [(source, (source + k) % tp_size) for source in range(tp_size)]
        weight_pieces.append(lax.ppermute(weight_piece((tp_index + k) % tp_size), "tp", pairs))

    own_kv = jnp.concatenate([key_proj, value_proj], axis=1)
    half = REACH // 2
    same_core = [shifted(own_kv, "ctx", 2 * (i + 1)) for i in range(half)]
    stack = jnp.concatenate([own_kv] + same_core, axis=0)
    parity = my_index % 2
    sibling = [(source, source ^ 1) for source in range(lax.axis_size("ctx"))]
    outgoing = lax.dynamic_slice_in_dim(stack, parity * tok_rows, half * tok_rows, 0)
    other_core = lax.ppermute(outgoing, "ctx", sibling)
    window_kv = jnp.concatenate([stack[tok_rows:], other_core, own_kv], axis=0)
    offsets = [2 * (i + 1) for i in range(half)] + [2 * i + 1 for i in range(half)] + [0]
    keys_three = window_kv[:, :kv_cols].reshape(window, heads_kv, HD)
    values_three = window_kv[:, kv_cols:].reshape(window, heads_kv, HD)

    query_four = queries.reshape(tok_rows, heads_kv, group_size, HD)
    grad_four = grad_out.reshape(tok_rows, heads_kv, group_size, HD)
    query_pos = my_index * tok_rows + jnp.arange(tok_rows, dtype=jnp.int32)
    block_pos = jnp.concatenate(
        [jnp.full((tok_rows,), offset, jnp.int32) for offset in offsets]
    )
    key_pos = (my_index * tok_rows - block_pos * tok_rows) + jnp.tile(
        jnp.arange(tok_rows, dtype=jnp.int32), blocks
    )
    visible = (key_pos[None, :] <= query_pos[:, None]) & (key_pos[None, :] >= doc_start[:, None])

    scores = (
        jnp.einsum("qkgd,pkd->kgqp", query_four, keys_three, preferred_element_type=jnp.float32)
        * soft_scale
    )
    scores = jnp.where(visible, scores, NEGATIVE)
    rowmax = jnp.max(scores, axis=-1)
    expw = jnp.exp(scores - rowmax[..., None])
    row_total = jnp.sum(expw, axis=-1)
    acc_sum = jnp.einsum(
        "kgqp,pkd->kgqd",
        expw.astype(jnp.bfloat16),
        values_three,
        preferred_element_type=jnp.float32,
    )
    attn_out = (acc_sum / row_total[..., None]).astype(jnp.bfloat16)
    log_total = rowmax + jnp.log(row_total)
    delta = jnp.einsum("qkgd,kgqd->kgq", grad_four, attn_out, preferred_element_type=jnp.float32)

    probs = jnp.exp(scores - log_total[..., None])
    value_part = jnp.einsum(
        "kgqp,qkgd->pkd", probs.astype(jnp.bfloat16), grad_four, preferred_element_type=jnp.float32
    )
    grad_probs = jnp.einsum(
        "qkgd,pkd->kgqp", grad_four, values_three, preferred_element_type=jnp.float32
    )
    grad_scores = (probs * (grad_probs - delta[..., None])).astype(jnp.bfloat16)
    query_part = (
        jnp.einsum("kgqp,pkd->qkgd", grad_scores, keys_three, preferred_element_type=jnp.float32)
        * soft_scale
    )
    key_part = (
        jnp.einsum("kgqp,qkgd->pkd", grad_scores, query_four, preferred_element_type=jnp.float32)
        * soft_scale
    )
    grad_query = query_part.reshape(tok_rows, heads_kv * group_size * HD).astype(jnp.bfloat16)

    partial_kv = jnp.concatenate(
        [key_part.reshape(window, kv_cols), value_part.reshape(window, kv_cols)], axis=1
    )
    span = half * tok_rows
    from_other = lax.ppermute(partial_kv[span : 2 * span].astype(jnp.bfloat16), "ctx", sibling)
    back_stack = jnp.concatenate([partial_kv[2 * span :], partial_kv[:span]], axis=0)
    back_stack = lax.dynamic_update_slice_in_dim(
        back_stack,
        lax.dynamic_slice_in_dim(back_stack, parity * tok_rows, span, 0)
        + from_other.astype(jnp.float32),
        parity * tok_rows,
        0,
    )
    total_kv = back_stack[:tok_rows]
    for i in range(half):
        piece = back_stack[(i + 1) * tok_rows : (i + 2) * tok_rows].astype(jnp.bfloat16)
        total_kv = total_kv + shifted(piece, "ctx", -2 * (i + 1)).astype(jnp.float32)
    grad_key = total_kv[:, :kv_cols].astype(jnp.bfloat16)
    grad_value = total_kv[:, kv_cols:].astype(jnp.bfloat16)
    own_grads = jnp.concatenate([grad_key, grad_value], axis=1)
    late_pieces, own_grads = lax.optimization_barrier((weight_pieces[1:], own_grads))

    total_input = jnp.einsum("rc,dc->rd", own_grads, own_rows, preferred_element_type=jnp.float32)
    for k in range(1, tp_size):
        pairs = [(source, (source + k) % tp_size) for source in range(tp_size)]
        their_grads = lax.ppermute(own_grads, "tp", pairs)
        total_input = total_input + jnp.einsum(
            "rc,dc->rd", their_grads, late_pieces[k - 1], preferred_element_type=jnp.float32
        )
    grad_input = total_input.astype(jnp.bfloat16)
    return (grad_query, grad_key, grad_value, grad_input)


def solution(mesh):
    in_specs = (
        P("ctx", "tp"),
        P("ctx", "tp"),
        P("ctx", "tp"),
        P("ctx", "tp"),
        P(None, "tp"),
        P(None, "tp"),
        P("ctx"),
    )
    out_specs = (P("ctx", "tp"), P("ctx", "tp"), P("ctx", "tp"), P("ctx", "tp"))
    return jax.shard_map(shards, mesh=mesh, in_specs=in_specs, out_specs=out_specs, check_vma=False)
```

```python
import math

import jax
import jax.numpy as jnp
from jax import lax
from jax.sharding import PartitionSpec as P

HEADS = 64
KV_HEADS = 8
HD = 128
REACH = 16


NEGATIVE = -1e30


def shifted(value, axis, steps):
    count = lax.axis_size(axis)
    pairs = [(source, (source + steps) % count) for source in range(count)]
    return lax.ppermute(value, axis, pairs)


def shards(queries, key_proj, value_proj, grad_out, key_weight, value_weight, doc_start):
    tok_rows = queries.shape[0]
    heads_kv = key_proj.shape[1] // HD
    kv_cols = key_proj.shape[1]
    group_size = HEADS // KV_HEADS
    soft_scale = 1.0 / math.sqrt(HD)
    my_index = lax.axis_index("ctx")
    blocks = REACH + 1
    window = blocks * tok_rows

    tp_size = lax.axis_size("tp")
    tp_index = lax.axis_index("tp")
    d_rows = key_weight.shape[0] // tp_size

    def weight_piece(target):
        return jnp.concatenate(
            [
                lax.dynamic_slice_in_dim(key_weight, target * d_rows, d_rows, 0),
                lax.dynamic_slice_in_dim(value_weight, target * d_rows, d_rows, 0),
            ],
            axis=1,
        )

    own_rows = weight_piece(tp_index)
    weight_pieces = [None]
    for k in range(1, tp_size):
        pairs = [(source, (source + k) % tp_size) for source in range(tp_size)]
        weight_pieces.append(lax.ppermute(weight_piece((tp_index + k) % tp_size), "tp", pairs))

    own_kv = jnp.concatenate([key_proj, value_proj], axis=1)
    half = REACH // 2
    same_core = [shifted(own_kv, "ctx", 2 * (i + 1)) for i in range(half)]
    stack = jnp.concatenate([own_kv] + same_core, axis=0)
    parity = my_index % 2
    sibling = [(source, source ^ 1) for source in range(lax.axis_size("ctx"))]
    outgoing = lax.dynamic_slice_in_dim(stack, parity * tok_rows, half * tok_rows, 0)
    other_core = lax.ppermute(outgoing, "ctx", sibling)
    window_kv = jnp.concatenate([stack[tok_rows:], other_core, own_kv], axis=0)
    offsets = [2 * (i + 1) for i in range(half)] + [2 * i + 1 for i in range(half)] + [0]
    keys_three = window_kv[:, :kv_cols].reshape(window, heads_kv, HD)
    values_three = window_kv[:, kv_cols:].reshape(window, heads_kv, HD)

    query_four = queries.reshape(tok_rows, heads_kv, group_size, HD)
    grad_four = grad_out.reshape(tok_rows, heads_kv, group_size, HD)
    query_pos = my_index * tok_rows + jnp.arange(tok_rows, dtype=jnp.int32)
    block_pos = jnp.concatenate(
        [jnp.full((tok_rows,), offset, jnp.int32) for offset in offsets]
    )
    key_pos = (my_index * tok_rows - block_pos * tok_rows) + jnp.tile(
        jnp.arange(tok_rows, dtype=jnp.int32), blocks
    )
    visible = (key_pos[None, :] <= query_pos[:, None]) & (key_pos[None, :] >= doc_start[:, None])

    scores = (
        jnp.einsum("qkgd,pkd->kgqp", query_four, keys_three, preferred_element_type=jnp.float32)
        * soft_scale
    )
    scores = jnp.where(visible, scores, NEGATIVE)
    rowmax = jnp.max(scores, axis=-1)
    expw = jnp.exp(scores - rowmax[..., None])
    row_total = jnp.sum(expw, axis=-1)
    acc_sum = jnp.einsum(
        "kgqp,pkd->kgqd",
        expw.astype(jnp.bfloat16),
        values_three,
        preferred_element_type=jnp.float32,
    )
    attn_out = (acc_sum / row_total[..., None]).astype(jnp.bfloat16)
    log_total = rowmax + jnp.log(row_total)
    delta = jnp.einsum("qkgd,kgqd->kgq", grad_four, attn_out, preferred_element_type=jnp.float32)

    probs = jnp.exp(scores - log_total[..., None])
    value_part = jnp.einsum(
        "kgqp,qkgd->pkd", probs.astype(jnp.bfloat16), grad_four, preferred_element_type=jnp.float32
    )
    grad_probs = jnp.einsum(
        "qkgd,pkd->kgqp", grad_four, values_three, preferred_element_type=jnp.float32
    )
    grad_scores = (probs * (grad_probs - delta[..., None])).astype(jnp.bfloat16)
    query_part = (
        jnp.einsum("kgqp,pkd->qkgd", grad_scores, keys_three, preferred_element_type=jnp.float32)
        * soft_scale
    )
    key_part = (
        jnp.einsum("kgqp,qkgd->pkd", grad_scores, query_four, preferred_element_type=jnp.float32)
        * soft_scale
    )
    grad_query = query_part.reshape(tok_rows, heads_kv * group_size * HD).astype(jnp.bfloat16)

    partial_kv = jnp.concatenate(
        [key_part.reshape(window, kv_cols), value_part.reshape(window, kv_cols)], axis=1
    )
    span = half * tok_rows
    from_other = lax.ppermute(partial_kv[span : 2 * span].astype(jnp.bfloat16), "ctx", sibling)
    back_stack = jnp.concatenate([partial_kv[2 * span :], partial_kv[:span]], axis=0)
    back_stack = lax.dynamic_update_slice_in_dim(
        back_stack,
        lax.dynamic_slice_in_dim(back_stack, parity * tok_rows, span, 0)
        + from_other.astype(jnp.float32),
        parity * tok_rows,
        0,
    )
    total_kv = back_stack[:tok_rows]
    for i in range(half):
        piece = back_stack[(i + 1) * tok_rows : (i + 2) * tok_rows].astype(jnp.bfloat16)
        total_kv = total_kv + shifted(piece, "ctx", -2 * (i + 1)).astype(jnp.float32)
    grad_key = total_kv[:, :kv_cols].astype(jnp.bfloat16)
    grad_value = total_kv[:, kv_cols:].astype(jnp.bfloat16)
    own_grads = jnp.concatenate([grad_key, grad_value], axis=1)
    late_pieces, own_grads = lax.optimization_barrier((weight_pieces[1:], own_grads))

    total_input = jnp.einsum("rc,dc->rd", own_grads, own_rows, preferred_element_type=jnp.float32)
    for k in range(1, tp_size):
        pairs = [(source, (source + k) % tp_size) for source in range(tp_size)]
        their_grads = lax.ppermute(own_grads, "tp", pairs)
        total_input = total_input + jnp.einsum(
            "rc,dc->rd", their_grads, late_pieces[k - 1], preferred_element_type=jnp.float32
        )
    grad_input = total_input.astype(jnp.bfloat16)
    return (grad_query, grad_key, grad_value, grad_input)


def solution(mesh):
    in_specs = (
        P("ctx", "tp"),
        P("ctx", "tp"),
        P("ctx", "tp"),
        P("ctx", "tp"),
        P(None, "tp"),
        P(None, "tp"),
        P("ctx"),
    )
    out_specs = (P("ctx", "tp"), P("ctx", "tp"), P("ctx", "tp"), P("ctx", "tp"))
    return jax.shard_map(shards, mesh=mesh, in_specs=in_specs, out_specs=out_specs, check_vma=False)
```

```python
import math

import jax
import jax.numpy as jnp
from jax import lax
from jax.sharding import PartitionSpec as P

HEADS = 64
KV_HEADS = 8
HD = 128
REACH = 16


NEGATIVE = -1e30


def shifted(value, axis, steps):
    count = lax.axis_size(axis)
    pairs = [(source, (source + steps) % count) for source in range(count)]
    return lax.ppermute(value, axis, pairs)


def shards(queries, key_proj, value_proj, grad_out, key_weight, value_weight, doc_start):
    tok_rows = queries.shape[0]
    heads_kv = key_proj.shape[1] // HD
    kv_cols = key_proj.shape[1]
    group_size = HEADS // KV_HEADS
    soft_scale = 1.0 / math.sqrt(HD)
    my_index = lax.axis_index("ctx")
    blocks = REACH + 1
    window = blocks * tok_rows

    tp_size = lax.axis_size("tp")
    tp_index = lax.axis_index("tp")
    own_kv = jnp.concatenate([key_proj, value_proj], axis=1)
    half = REACH // 2
    same_core = [shifted(own_kv, "ctx", 2 * (i + 1)) for i in range(half)]
    stack = jnp.concatenate([own_kv] + same_core, axis=0)
    parity = my_index % 2
    sibling = [(source, source ^ 1) for source in range(lax.axis_size("ctx"))]
    outgoing = lax.dynamic_slice_in_dim(stack, parity * tok_rows, half * tok_rows, 0)
    other_core = lax.ppermute(outgoing, "ctx", sibling)
    window_kv = jnp.concatenate([stack[tok_rows:], other_core, own_kv], axis=0)
    offsets = [2 * (i + 1) for i in range(half)] + [2 * i + 1 for i in range(half)] + [0]
    keys_three = window_kv[:, :kv_cols].reshape(window, heads_kv, HD)
    values_three = window_kv[:, kv_cols:].reshape(window, heads_kv, HD)

    query_four = queries.reshape(tok_rows, heads_kv, group_size, HD)
    grad_four = grad_out.reshape(tok_rows, heads_kv, group_size, HD)
    query_pos = my_index * tok_rows + jnp.arange(tok_rows, dtype=jnp.int32)
    block_pos = jnp.concatenate(
        [jnp.full((tok_rows,), offset, jnp.int32) for offset in offsets]
    )
    key_pos = (my_index * tok_rows - block_pos * tok_rows) + jnp.tile(
        jnp.arange(tok_rows, dtype=jnp.int32), blocks
    )
    visible = (key_pos[None, :] <= query_pos[:, None]) & (key_pos[None, :] >= doc_start[:, None])

    scores = (
        jnp.einsum("qkgd,pkd->kgqp", query_four, keys_three, preferred_element_type=jnp.float32)
        * soft_scale
    )
    scores = jnp.where(visible, scores, NEGATIVE)
    rowmax = jnp.max(scores, axis=-1)
    expw = jnp.exp(scores - rowmax[..., None])
    row_total = jnp.sum(expw, axis=-1)
    acc_sum = jnp.einsum(
        "kgqp,pkd->kgqd",
        expw.astype(jnp.bfloat16),
        values_three,
        preferred_element_type=jnp.float32,
    )
    attn_out = (acc_sum / row_total[..., None]).astype(jnp.bfloat16)
    log_total = rowmax + jnp.log(row_total)
    delta = jnp.einsum("qkgd,kgqd->kgq", grad_four, attn_out, preferred_element_type=jnp.float32)

    probs = jnp.exp(scores - log_total[..., None])
    value_part = jnp.einsum(
        "kgqp,qkgd->pkd", probs.astype(jnp.bfloat16), grad_four, preferred_element_type=jnp.float32
    )
    grad_probs = jnp.einsum(
        "qkgd,pkd->kgqp", grad_four, values_three, preferred_element_type=jnp.float32
    )
    grad_scores = (probs * (grad_probs - delta[..., None])).astype(jnp.bfloat16)
    query_part = (
        jnp.einsum("kgqp,pkd->qkgd", grad_scores, keys_three, preferred_element_type=jnp.float32)
        * soft_scale
    )
    key_part = (
        jnp.einsum("kgqp,qkgd->pkd", grad_scores, query_four, preferred_element_type=jnp.float32)
        * soft_scale
    )
    grad_query = query_part.reshape(tok_rows, heads_kv * group_size * HD).astype(jnp.bfloat16)

    partial_kv = jnp.concatenate(
        [key_part.reshape(window, kv_cols), value_part.reshape(window, kv_cols)], axis=1
    )
    span = half * tok_rows
    from_other = lax.ppermute(partial_kv[span : 2 * span].astype(jnp.bfloat16), "ctx", sibling)
    back_stack = jnp.concatenate([partial_kv[2 * span :], partial_kv[:span]], axis=0)
    back_stack = lax.dynamic_update_slice_in_dim(
        back_stack,
        lax.dynamic_slice_in_dim(back_stack, parity * tok_rows, span, 0)
        + from_other.astype(jnp.float32),
        parity * tok_rows,
        0,
    )
    total_kv = back_stack[:tok_rows]
    for i in range(half):
        piece = back_stack[(i + 1) * tok_rows : (i + 2) * tok_rows].astype(jnp.bfloat16)
        total_kv = total_kv + shifted(piece, "ctx", -2 * (i + 1)).astype(jnp.float32)
    grad_key = total_kv[:, :kv_cols].astype(jnp.bfloat16)
    grad_value = total_kv[:, kv_cols:].astype(jnp.bfloat16)
    d_rows = key_weight.shape[0] // tp_size
    partial_input = jnp.einsum(
        "rc,jdc->jrd",
        grad_key,
        key_weight.reshape(tp_size, d_rows, kv_cols),
        preferred_element_type=jnp.float32,
    ) + jnp.einsum(
        "rc,jdc->jrd",
        grad_value,
        value_weight.reshape(tp_size, d_rows, kv_cols),
        preferred_element_type=jnp.float32,
    )
    received = lax.all_to_all(partial_input.astype(jnp.bfloat16), "tp", 0, 0, tiled=True)
    grad_input = jnp.sum(received.astype(jnp.float32), axis=0).astype(jnp.bfloat16)
    return (grad_query, grad_key, grad_value, grad_input)


def solution(mesh):
    in_specs = (
        P("ctx", "tp"),
        P("ctx", "tp"),
        P("ctx", "tp"),
        P("ctx", "tp"),
        P(None, "tp"),
        P(None, "tp"),
        P("ctx"),
    )
    out_specs = (P("ctx", "tp"), P("ctx", "tp"), P("ctx", "tp"), P("ctx", "tp"))
    return jax.shard_map(shards, mesh=mesh, in_specs=in_specs, out_specs=out_specs, check_vma=False)
```

```python
import math

import jax
import jax.numpy as jnp
from jax import lax
from jax.sharding import PartitionSpec as P

HEADS = 64
KV_HEADS = 8
HD = 128


NEGATIVE = -1e30


def shifted(value, axis, steps):
    count = lax.axis_size(axis)
    pairs = [(source, (source + steps) % count) for source in range(count)]
    return lax.ppermute(value, axis, pairs)


def shards(queries, key_proj, value_proj, grad_out, key_weight, value_weight, doc_start):
    tok_rows = queries.shape[0]
    heads_kv = key_proj.shape[1] // HD
    kv_cols = key_proj.shape[1]
    group_size = HEADS // KV_HEADS
    soft_scale = 1.0 / math.sqrt(HD)
    my_index = lax.axis_index("ctx")

    tp_size = lax.axis_size("tp")
    tp_index = lax.axis_index("tp")
    own_kv = jnp.concatenate([key_proj, value_proj], axis=1)
    parity = my_index % 2
    sibling = [(source, source ^ 1) for source in range(lax.axis_size("ctx"))]
    swapped = lax.ppermute(own_kv, "ctx", sibling)
    pair = jnp.where(
        parity == 0,
        jnp.concatenate([own_kv, swapped], axis=0),
        jnp.concatenate([swapped, own_kv], axis=0),
    )
    farthest = shifted(pair, "ctx", 2 * 8)
    level = pair
    for chips in (4, 2, 1):
        level = jnp.concatenate([level, shifted(level, "ctx", 2 * chips)], axis=0)
    window_kv = jnp.concatenate([level, farthest], axis=0)
    chip_offsets = [0, 4, 2, 6, 1, 5, 3, 7, 8]
    blocks = 2 * len(chip_offsets)
    window = blocks * tok_rows
    keys_three = window_kv[:, :kv_cols].reshape(window, heads_kv, HD)
    values_three = window_kv[:, kv_cols:].reshape(window, heads_kv, HD)

    query_four = queries.reshape(tok_rows, heads_kv, group_size, HD)
    grad_four = grad_out.reshape(tok_rows, heads_kv, group_size, HD)
    query_pos = my_index * tok_rows + jnp.arange(tok_rows, dtype=jnp.int32)
    block_of = jnp.concatenate(
        [
            jnp.full((tok_rows,), 2 * offset - core, jnp.int32)
            for offset in chip_offsets
            for core in (0, 1)
        ]
    )
    chip_first = my_index - parity
    key_pos = (chip_first - block_of) * tok_rows + jnp.tile(
        jnp.arange(tok_rows, dtype=jnp.int32), blocks
    )
    visible = (key_pos[None, :] <= query_pos[:, None]) & (key_pos[None, :] >= doc_start[:, None])

    scores = (
        jnp.einsum("qkgd,pkd->kgqp", query_four, keys_three, preferred_element_type=jnp.float32)
        * soft_scale
    )
    scores = jnp.where(visible, scores, NEGATIVE)
    rowmax = jnp.max(scores, axis=-1)
    expw = jnp.exp(scores - rowmax[..., None])
    row_total = jnp.sum(expw, axis=-1)
    acc_sum = jnp.einsum(
        "kgqp,pkd->kgqd",
        expw.astype(jnp.bfloat16),
        values_three,
        preferred_element_type=jnp.float32,
    )
    attn_out = (acc_sum / row_total[..., None]).astype(jnp.bfloat16)
    log_total = rowmax + jnp.log(row_total)
    delta = jnp.einsum("qkgd,kgqd->kgq", grad_four, attn_out, preferred_element_type=jnp.float32)

    probs = jnp.exp(scores - log_total[..., None])
    value_part = jnp.einsum(
        "kgqp,qkgd->pkd", probs.astype(jnp.bfloat16), grad_four, preferred_element_type=jnp.float32
    )
    grad_probs = jnp.einsum(
        "qkgd,pkd->kgqp", grad_four, values_three, preferred_element_type=jnp.float32
    )
    grad_scores = (probs * (grad_probs - delta[..., None])).astype(jnp.bfloat16)
    query_part = (
        jnp.einsum("kgqp,pkd->qkgd", grad_scores, keys_three, preferred_element_type=jnp.float32)
        * soft_scale
    )
    key_part = (
        jnp.einsum("kgqp,qkgd->pkd", grad_scores, query_four, preferred_element_type=jnp.float32)
        * soft_scale
    )
    grad_query = query_part.reshape(tok_rows, heads_kv * group_size * HD).astype(jnp.bfloat16)

    partial_kv = jnp.concatenate(
        [key_part.reshape(window, kv_cols), value_part.reshape(window, kv_cols)], axis=1
    )
    pair_rows = 2 * tok_rows
    from_farthest = shifted(partial_kv[8 * pair_rows :].astype(jnp.bfloat16), "ctx", -2 * 8)
    level = partial_kv[: 8 * pair_rows]
    for chips in (1, 2, 4):
        half_rows = level.shape[0] // 2
        back = shifted(level[half_rows:].astype(jnp.bfloat16), "ctx", -2 * chips)
        level = level[:half_rows] + back.astype(jnp.float32)
    level = level + from_farthest.astype(jnp.float32)
    mine = lax.dynamic_slice_in_dim(level, parity * tok_rows, tok_rows, 0)
    theirs = lax.dynamic_slice_in_dim(level, (1 - parity) * tok_rows, tok_rows, 0)
    total_kv = mine + lax.ppermute(theirs.astype(jnp.bfloat16), "ctx", sibling).astype(jnp.float32)
    grad_key = total_kv[:, :kv_cols].astype(jnp.bfloat16)
    grad_value = total_kv[:, kv_cols:].astype(jnp.bfloat16)
    d_rows = key_weight.shape[0] // tp_size
    partial_input = jnp.einsum(
        "rc,jdc->jrd",
        grad_key,
        key_weight.reshape(tp_size, d_rows, kv_cols),
        preferred_element_type=jnp.float32,
    ) + jnp.einsum(
        "rc,jdc->jrd",
        grad_value,
        value_weight.reshape(tp_size, d_rows, kv_cols),
        preferred_element_type=jnp.float32,
    )
    received = lax.all_to_all(partial_input.astype(jnp.bfloat16), "tp", 0, 0, tiled=True)
    grad_input = jnp.sum(received.astype(jnp.float32), axis=0).astype(jnp.bfloat16)
    return (grad_query, grad_key, grad_value, grad_input)


def solution(mesh):
    in_specs = (
        P("ctx", "tp"),
        P("ctx", "tp"),
        P("ctx", "tp"),
        P("ctx", "tp"),
        P(None, "tp"),
        P(None, "tp"),
        P("ctx"),
    )
    out_specs = (P("ctx", "tp"), P("ctx", "tp"), P("ctx", "tp"), P("ctx", "tp"))
    return jax.shard_map(shards, mesh=mesh, in_specs=in_specs, out_specs=out_specs, check_vma=False)
```

```python
import math

import jax
import jax.numpy as jnp
from jax import lax
from jax.sharding import PartitionSpec as P

HEADS = 64
KV_HEADS = 8
HD = 128
REACH = 16


NEGATIVE = -1e30


def shifted(value, axis, steps):
    count = lax.axis_size(axis)
    pairs = [(source, (source + steps) % count) for source in range(count)]
    return lax.ppermute(value, axis, pairs)


def shards(queries, key_proj, value_proj, grad_out, key_weight, value_weight, doc_start):
    tok_rows = queries.shape[0]
    heads_kv = key_proj.shape[1] // HD
    kv_cols = key_proj.shape[1]
    group_size = HEADS // KV_HEADS
    soft_scale = 1.0 / math.sqrt(HD)
    my_index = lax.axis_index("ctx")
    blocks = REACH + 1
    window = blocks * tok_rows

    tp_size = lax.axis_size("tp")
    tp_index = lax.axis_index("tp")
    d_rows = key_weight.shape[0] // tp_size
    key_rows = lax.all_to_all(key_weight.reshape(tp_size, d_rows, kv_cols), "tp", 0, 0, tiled=True)
    value_rows = lax.all_to_all(value_weight.reshape(tp_size, d_rows, kv_cols), "tp", 0, 0, tiled=True)

    own_kv = jnp.concatenate([key_proj, value_proj], axis=1)
    half = REACH // 2
    same_core = [shifted(own_kv, "ctx", 2 * (i + 1)) for i in range(half)]
    stack = jnp.concatenate([own_kv] + same_core, axis=0)
    parity = my_index % 2
    sibling = [(source, source ^ 1) for source in range(lax.axis_size("ctx"))]
    outgoing = lax.dynamic_slice_in_dim(stack, parity * tok_rows, half * tok_rows, 0)
    other_core = lax.ppermute(outgoing, "ctx", sibling)
    window_kv = jnp.concatenate([stack[tok_rows:], other_core, own_kv], axis=0)
    offsets = [2 * (i + 1) for i in range(half)] + [2 * i + 1 for i in range(half)] + [0]
    keys_three = window_kv[:, :kv_cols].reshape(window, heads_kv, HD)
    values_three = window_kv[:, kv_cols:].reshape(window, heads_kv, HD)

    query_four = queries.reshape(tok_rows, heads_kv, group_size, HD)
    grad_four = grad_out.reshape(tok_rows, heads_kv, group_size, HD)
    query_pos = my_index * tok_rows + jnp.arange(tok_rows, dtype=jnp.int32)
    block_pos = jnp.concatenate(
        [jnp.full((tok_rows,), offset, jnp.int32) for offset in offsets]
    )
    key_pos = (my_index * tok_rows - block_pos * tok_rows) + jnp.tile(
        jnp.arange(tok_rows, dtype=jnp.int32), blocks
    )
    visible = (key_pos[None, :] <= query_pos[:, None]) & (key_pos[None, :] >= doc_start[:, None])

    scores = (
        jnp.einsum("qkgd,pkd->kgqp", query_four, keys_three, preferred_element_type=jnp.float32)
        * soft_scale
    )
    scores = jnp.where(visible, scores, NEGATIVE)
    rowmax = jnp.max(scores, axis=-1)
    expw = jnp.exp(scores - rowmax[..., None])
    row_total = jnp.sum(expw, axis=-1)
    acc_sum = jnp.einsum(
        "kgqp,pkd->kgqd",
        expw.astype(jnp.bfloat16),
        values_three,
        preferred_element_type=jnp.float32,
    )
    attn_out = (acc_sum / row_total[..., None]).astype(jnp.bfloat16)
    log_total = rowmax + jnp.log(row_total)
    delta = jnp.einsum("qkgd,kgqd->kgq", grad_four, attn_out, preferred_element_type=jnp.float32)

    probs = jnp.exp(scores - log_total[..., None])
    value_part = jnp.einsum(
        "kgqp,qkgd->pkd", probs.astype(jnp.bfloat16), grad_four, preferred_element_type=jnp.float32
    )
    grad_probs = jnp.einsum(
        "qkgd,pkd->kgqp", grad_four, values_three, preferred_element_type=jnp.float32
    )
    grad_scores = (probs * (grad_probs - delta[..., None])).astype(jnp.bfloat16)
    query_part = (
        jnp.einsum("kgqp,pkd->qkgd", grad_scores, keys_three, preferred_element_type=jnp.float32)
        * soft_scale
    )
    key_part = (
        jnp.einsum("kgqp,qkgd->pkd", grad_scores, query_four, preferred_element_type=jnp.float32)
        * soft_scale
    )
    grad_query = query_part.reshape(tok_rows, heads_kv * group_size * HD).astype(jnp.bfloat16)

    partial_kv = jnp.concatenate(
        [key_part.reshape(window, kv_cols), value_part.reshape(window, kv_cols)], axis=1
    )
    span = half * tok_rows
    from_other = lax.ppermute(partial_kv[span : 2 * span].astype(jnp.bfloat16), "ctx", sibling)
    back_stack = jnp.concatenate([partial_kv[2 * span :], partial_kv[:span]], axis=0)
    back_stack = lax.dynamic_update_slice_in_dim(
        back_stack,
        lax.dynamic_slice_in_dim(back_stack, parity * tok_rows, span, 0)
        + from_other.astype(jnp.float32),
        parity * tok_rows,
        0,
    )
    total_kv = back_stack[:tok_rows]
    for i in range(half):
        piece = back_stack[(i + 1) * tok_rows : (i + 2) * tok_rows].astype(jnp.bfloat16)
        total_kv = total_kv + shifted(piece, "ctx", -2 * (i + 1)).astype(jnp.float32)
    grad_key = total_kv[:, :kv_cols].astype(jnp.bfloat16)
    grad_value = total_kv[:, kv_cols:].astype(jnp.bfloat16)
    own_grads = jnp.concatenate([grad_key, grad_value], axis=1)
    (key_rows, value_rows), own_grads = lax.optimization_barrier(((key_rows, value_rows), own_grads))
    every_grads = lax.all_to_all(
        jnp.broadcast_to(own_grads[None], (tp_size,) + own_grads.shape), "tp", 0, 0, tiled=True
    )
    grad_input = (
        jnp.einsum(
            "jrc,jdc->rd", every_grads[:, :, :kv_cols], key_rows, preferred_element_type=jnp.float32
        )
        + jnp.einsum(
            "jrc,jdc->rd", every_grads[:, :, kv_cols:], value_rows, preferred_element_type=jnp.float32
        )
    ).astype(jnp.bfloat16)
    return (grad_query, grad_key, grad_value, grad_input)


def solution(mesh):
    in_specs = (
        P("ctx", "tp"),
        P("ctx", "tp"),
        P("ctx", "tp"),
        P("ctx", "tp"),
        P(None, "tp"),
        P(None, "tp"),
        P("ctx"),
    )
    out_specs = (P("ctx", "tp"), P("ctx", "tp"), P("ctx", "tp"), P("ctx", "tp"))
    return jax.shard_map(shards, mesh=mesh, in_specs=in_specs, out_specs=out_specs, check_vma=False)
```

```python
import math

import jax
import jax.numpy as jnp
from jax import lax
from jax.sharding import PartitionSpec as P

HEADS = 64
KV_HEADS = 8
HD = 128
REACH = 16


NEGATIVE = -1e30


def shifted(value, axis, steps):
    count = lax.axis_size(axis)
    pairs = [(source, (source + steps) % count) for source in range(count)]
    return lax.ppermute(value, axis, pairs)


def shards(queries, key_proj, value_proj, grad_out, key_weight, value_weight, doc_start):
    tok_rows = queries.shape[0]
    heads_kv = key_proj.shape[1] // HD
    kv_cols = key_proj.shape[1]
    group_size = HEADS // KV_HEADS
    soft_scale = 1.0 / math.sqrt(HD)
    my_index = lax.axis_index("ctx")
    blocks = REACH + 1
    window = blocks * tok_rows

    tp_size = lax.axis_size("tp")
    tp_index = lax.axis_index("tp")
    d_rows = key_weight.shape[0] // tp_size
    both_rows = jnp.concatenate(
        [
            key_weight.reshape(tp_size, d_rows, kv_cols),
            value_weight.reshape(tp_size, d_rows, kv_cols),
        ],
        axis=2,
    )
    both_rows = lax.all_to_all(both_rows, "tp", 0, 0, tiled=True)

    own_kv = jnp.concatenate([key_proj, value_proj], axis=1)
    half = REACH // 2
    same_core = [shifted(own_kv, "ctx", 2 * (i + 1)) for i in range(half)]
    stack = jnp.concatenate([own_kv] + same_core, axis=0)
    parity = my_index % 2
    sibling = [(source, source ^ 1) for source in range(lax.axis_size("ctx"))]
    outgoing = lax.dynamic_slice_in_dim(stack, parity * tok_rows, half * tok_rows, 0)
    other_core = lax.ppermute(outgoing, "ctx", sibling)
    window_kv = jnp.concatenate([stack[tok_rows:], other_core, own_kv], axis=0)
    offsets = [2 * (i + 1) for i in range(half)] + [2 * i + 1 for i in range(half)] + [0]
    keys_three = window_kv[:, :kv_cols].reshape(window, heads_kv, HD)
    values_three = window_kv[:, kv_cols:].reshape(window, heads_kv, HD)

    query_four = queries.reshape(tok_rows, heads_kv, group_size, HD)
    grad_four = grad_out.reshape(tok_rows, heads_kv, group_size, HD)
    query_pos = my_index * tok_rows + jnp.arange(tok_rows, dtype=jnp.int32)
    block_pos = jnp.concatenate(
        [jnp.full((tok_rows,), offset, jnp.int32) for offset in offsets]
    )
    key_pos = (my_index * tok_rows - block_pos * tok_rows) + jnp.tile(
        jnp.arange(tok_rows, dtype=jnp.int32), blocks
    )
    visible = (key_pos[None, :] <= query_pos[:, None]) & (key_pos[None, :] >= doc_start[:, None])

    scores = (
        jnp.einsum("qkgd,pkd->kgqp", query_four, keys_three, preferred_element_type=jnp.float32)
        * soft_scale
    )
    scores = jnp.where(visible, scores, NEGATIVE)
    rowmax = jnp.max(scores, axis=-1)
    expw = jnp.exp(scores - rowmax[..., None])
    row_total = jnp.sum(expw, axis=-1)
    acc_sum = jnp.einsum(
        "kgqp,pkd->kgqd",
        expw.astype(jnp.bfloat16),
        values_three,
        preferred_element_type=jnp.float32,
    )
    attn_out = (acc_sum / row_total[..., None]).astype(jnp.bfloat16)
    log_total = rowmax + jnp.log(row_total)
    delta = jnp.einsum("qkgd,kgqd->kgq", grad_four, attn_out, preferred_element_type=jnp.float32)

    probs = jnp.exp(scores - log_total[..., None])
    value_part = jnp.einsum(
        "kgqp,qkgd->pkd", probs.astype(jnp.bfloat16), grad_four, preferred_element_type=jnp.float32
    )
    grad_probs = jnp.einsum(
        "qkgd,pkd->kgqp", grad_four, values_three, preferred_element_type=jnp.float32
    )
    grad_scores = (probs * (grad_probs - delta[..., None])).astype(jnp.bfloat16)
    query_part = (
        jnp.einsum("kgqp,pkd->qkgd", grad_scores, keys_three, preferred_element_type=jnp.float32)
        * soft_scale
    )
    key_part = (
        jnp.einsum("kgqp,qkgd->pkd", grad_scores, query_four, preferred_element_type=jnp.float32)
        * soft_scale
    )
    grad_query = query_part.reshape(tok_rows, heads_kv * group_size * HD).astype(jnp.bfloat16)

    partial_kv = jnp.concatenate(
        [key_part.reshape(window, kv_cols), value_part.reshape(window, kv_cols)], axis=1
    )
    span = half * tok_rows
    from_other = lax.ppermute(partial_kv[span : 2 * span].astype(jnp.bfloat16), "ctx", sibling)
    back_stack = jnp.concatenate([partial_kv[2 * span :], partial_kv[:span]], axis=0)
    back_stack = lax.dynamic_update_slice_in_dim(
        back_stack,
        lax.dynamic_slice_in_dim(back_stack, parity * tok_rows, span, 0)
        + from_other.astype(jnp.float32),
        parity * tok_rows,
        0,
    )
    total_kv = back_stack[:tok_rows]
    for i in range(half):
        piece = back_stack[(i + 1) * tok_rows : (i + 2) * tok_rows].astype(jnp.bfloat16)
        total_kv = total_kv + shifted(piece, "ctx", -2 * (i + 1)).astype(jnp.float32)
    grad_key = total_kv[:, :kv_cols].astype(jnp.bfloat16)
    grad_value = total_kv[:, kv_cols:].astype(jnp.bfloat16)
    own_grads = jnp.concatenate([grad_key, grad_value], axis=1)
    both_rows, own_grads = lax.optimization_barrier((both_rows, own_grads))
    every_grads = lax.all_to_all(
        jnp.broadcast_to(own_grads[None], (tp_size,) + own_grads.shape), "tp", 0, 0, tiled=True
    )
    grad_input = jnp.einsum(
        "jrc,jdc->rd", every_grads, both_rows, preferred_element_type=jnp.float32
    ).astype(jnp.bfloat16)
    return (grad_query, grad_key, grad_value, grad_input)


def solution(mesh):
    in_specs = (
        P("ctx", "tp"),
        P("ctx", "tp"),
        P("ctx", "tp"),
        P("ctx", "tp"),
        P(None, "tp"),
        P(None, "tp"),
        P("ctx"),
    )
    out_specs = (P("ctx", "tp"), P("ctx", "tp"), P("ctx", "tp"), P("ctx", "tp"))
    return jax.shard_map(shards, mesh=mesh, in_specs=in_specs, out_specs=out_specs, check_vma=False)
```

```python
import math

import jax
import jax.numpy as jnp
from jax import lax
from jax.sharding import PartitionSpec as P

HEADS = 64
KV_HEADS = 8
HD = 128
REACH = 16


NEGATIVE = -1e30


def shifted(value, axis, steps):
    count = lax.axis_size(axis)
    pairs = [(source, (source + steps) % count) for source in range(count)]
    return lax.ppermute(value, axis, pairs)


def shards(queries, key_proj, value_proj, grad_out, key_weight, value_weight, doc_start):
    tok_rows = queries.shape[0]
    heads_kv = key_proj.shape[1] // HD
    kv_cols = key_proj.shape[1]
    group_size = HEADS // KV_HEADS
    soft_scale = 1.0 / math.sqrt(HD)
    my_index = lax.axis_index("ctx")
    blocks = REACH + 1
    window = blocks * tok_rows

    tp_size = lax.axis_size("tp")
    tp_index = lax.axis_index("tp")
    d_rows = key_weight.shape[0] // tp_size
    both_rows = jnp.concatenate(
        [
            key_weight.reshape(tp_size, d_rows, kv_cols),
            value_weight.reshape(tp_size, d_rows, kv_cols),
        ],
        axis=2,
    )
    both_rows = lax.all_to_all(both_rows, "tp", 0, 0, tiled=True)

    own_kv = jnp.concatenate([key_proj, value_proj], axis=1)
    half = REACH // 2
    same_core = [shifted(own_kv, "ctx", 2 * (i + 1)) for i in range(half)]
    stack = jnp.concatenate([own_kv] + same_core, axis=0)
    parity = my_index % 2
    sibling = [(source, source ^ 1) for source in range(lax.axis_size("ctx"))]
    outgoing = lax.dynamic_slice_in_dim(stack, parity * tok_rows, half * tok_rows, 0)
    other_core = lax.ppermute(outgoing, "ctx", sibling)
    window_kv = jnp.concatenate([stack[tok_rows:], other_core, own_kv], axis=0)
    offsets = [2 * (i + 1) for i in range(half)] + [2 * i + 1 for i in range(half)] + [0]
    keys_three = window_kv[:, :kv_cols].reshape(window, heads_kv, HD)
    values_three = window_kv[:, kv_cols:].reshape(window, heads_kv, HD)

    query_four = queries.reshape(tok_rows, heads_kv, group_size, HD)
    grad_four = grad_out.reshape(tok_rows, heads_kv, group_size, HD)
    query_pos = my_index * tok_rows + jnp.arange(tok_rows, dtype=jnp.int32)
    block_pos = jnp.concatenate(
        [jnp.full((tok_rows,), offset, jnp.int32) for offset in offsets]
    )
    key_pos = (my_index * tok_rows - block_pos * tok_rows) + jnp.tile(
        jnp.arange(tok_rows, dtype=jnp.int32), blocks
    )
    visible = (key_pos[None, :] <= query_pos[:, None]) & (key_pos[None, :] >= doc_start[:, None])

    scores = (
        jnp.einsum("qkgd,pkd->kgqp", query_four, keys_three, preferred_element_type=jnp.float32)
        * soft_scale
    )
    scores = jnp.where(visible, scores, NEGATIVE)
    rowmax = jnp.max(scores, axis=-1)
    expw = jnp.exp(scores - rowmax[..., None])
    row_total = jnp.sum(expw, axis=-1)
    acc_sum = jnp.einsum(
        "kgqp,pkd->kgqd",
        expw.astype(jnp.bfloat16),
        values_three,
        preferred_element_type=jnp.float32,
    )
    attn_out = (acc_sum / row_total[..., None]).astype(jnp.bfloat16)
    log_total = rowmax + jnp.log(row_total)
    delta = jnp.einsum("qkgd,kgqd->kgq", grad_four, attn_out, preferred_element_type=jnp.float32)

    probs = jnp.exp(scores - log_total[..., None])
    value_part = jnp.einsum(
        "kgqp,qkgd->pkd", probs.astype(jnp.bfloat16), grad_four, preferred_element_type=jnp.float32
    )
    grad_probs = jnp.einsum(
        "qkgd,pkd->kgqp", grad_four, values_three, preferred_element_type=jnp.float32
    )
    grad_scores = (probs * (grad_probs - delta[..., None])).astype(jnp.bfloat16)
    query_part = (
        jnp.einsum("kgqp,pkd->qkgd", grad_scores, keys_three, preferred_element_type=jnp.float32)
        * soft_scale
    )
    key_part = (
        jnp.einsum("kgqp,qkgd->pkd", grad_scores, query_four, preferred_element_type=jnp.float32)
        * soft_scale
    )
    grad_query = query_part.reshape(tok_rows, heads_kv * group_size * HD).astype(jnp.bfloat16)

    partial_kv = jnp.concatenate(
        [key_part.reshape(window, kv_cols), value_part.reshape(window, kv_cols)], axis=1
    )
    span = half * tok_rows
    from_other = lax.ppermute(partial_kv[span : 2 * span].astype(jnp.bfloat16), "ctx", sibling)
    back_stack = jnp.concatenate([partial_kv[2 * span :], partial_kv[:span]], axis=0)
    back_stack = lax.dynamic_update_slice_in_dim(
        back_stack,
        lax.dynamic_slice_in_dim(back_stack, parity * tok_rows, span, 0)
        + from_other.astype(jnp.float32),
        parity * tok_rows,
        0,
    )
    total_kv = back_stack[:tok_rows]
    for i in reversed(range(half)):
        piece = back_stack[(i + 1) * tok_rows : (i + 2) * tok_rows].astype(jnp.bfloat16)
        total_kv = total_kv + shifted(piece, "ctx", -2 * (i + 1)).astype(jnp.float32)
    grad_key = total_kv[:, :kv_cols].astype(jnp.bfloat16)
    grad_value = total_kv[:, kv_cols:].astype(jnp.bfloat16)
    own_grads = jnp.concatenate([grad_key, grad_value], axis=1)
    both_rows, own_grads = lax.optimization_barrier((both_rows, own_grads))
    every_grads = lax.all_to_all(
        jnp.broadcast_to(own_grads[None], (tp_size,) + own_grads.shape), "tp", 0, 0, tiled=True
    )
    grad_input = jnp.einsum(
        "jrc,jdc->rd", every_grads, both_rows, preferred_element_type=jnp.float32
    ).astype(jnp.bfloat16)
    return (grad_query, grad_key, grad_value, grad_input)


def solution(mesh):
    in_specs = (
        P("ctx", "tp"),
        P("ctx", "tp"),
        P("ctx", "tp"),
        P("ctx", "tp"),
        P(None, "tp"),
        P(None, "tp"),
        P("ctx"),
    )
    out_specs = (P("ctx", "tp"), P("ctx", "tp"), P("ctx", "tp"), P("ctx", "tp"))
    return jax.shard_map(shards, mesh=mesh, in_specs=in_specs, out_specs=out_specs, check_vma=False)
```

```python
import math

import jax
import jax.numpy as jnp
from jax import lax
from jax.sharding import PartitionSpec as P

HEADS = 64
KV_HEADS = 8
HD = 128
REACH = 16


NEGATIVE = -1e30


def shifted(value, axis, steps):
    count = lax.axis_size(axis)
    pairs = [(source, (source + steps) % count) for source in range(count)]
    return lax.ppermute(value, axis, pairs)


def shards(queries, key_proj, value_proj, grad_out, key_weight, value_weight, doc_start):
    tok_rows = queries.shape[0]
    heads_kv = key_proj.shape[1] // HD
    kv_cols = key_proj.shape[1]
    group_size = HEADS // KV_HEADS
    soft_scale = 1.0 / math.sqrt(HD)
    my_index = lax.axis_index("ctx")
    blocks = REACH + 1
    window = blocks * tok_rows

    tp_size = lax.axis_size("tp")
    tp_index = lax.axis_index("tp")
    d_rows = key_weight.shape[0] // tp_size
    both_rows = jnp.stack(
        [
            key_weight.reshape(tp_size, d_rows, kv_cols),
            value_weight.reshape(tp_size, d_rows, kv_cols),
        ],
        axis=1,
    )
    both_rows = lax.all_to_all(both_rows, "tp", 0, 0, tiled=True)

    own_kv = jnp.concatenate([key_proj, value_proj], axis=1)
    half = REACH // 2
    same_core = [shifted(own_kv, "ctx", 2 * (i + 1)) for i in range(half)]
    stack = jnp.concatenate([own_kv] + same_core, axis=0)
    parity = my_index % 2
    sibling = [(source, source ^ 1) for source in range(lax.axis_size("ctx"))]
    outgoing = lax.dynamic_slice_in_dim(stack, parity * tok_rows, half * tok_rows, 0)
    other_core = lax.ppermute(outgoing, "ctx", sibling)
    window_kv = jnp.concatenate([stack[tok_rows:], other_core, own_kv], axis=0)
    offsets = [2 * (i + 1) for i in range(half)] + [2 * i + 1 for i in range(half)] + [0]
    keys_three = window_kv[:, :kv_cols].reshape(window, heads_kv, HD)
    values_three = window_kv[:, kv_cols:].reshape(window, heads_kv, HD)

    query_four = queries.reshape(tok_rows, heads_kv, group_size, HD)
    grad_four = grad_out.reshape(tok_rows, heads_kv, group_size, HD)
    query_pos = my_index * tok_rows + jnp.arange(tok_rows, dtype=jnp.int32)
    block_pos = jnp.concatenate(
        [jnp.full((tok_rows,), offset, jnp.int32) for offset in offsets]
    )
    key_pos = (my_index * tok_rows - block_pos * tok_rows) + jnp.tile(
        jnp.arange(tok_rows, dtype=jnp.int32), blocks
    )
    visible = (key_pos[None, :] <= query_pos[:, None]) & (key_pos[None, :] >= doc_start[:, None])

    scores = (
        jnp.einsum("qkgd,pkd->kgqp", query_four, keys_three, preferred_element_type=jnp.float32)
        * soft_scale
    )
    scores = jnp.where(visible, scores, NEGATIVE)
    rowmax = jnp.max(scores, axis=-1)
    expw = jnp.exp(scores - rowmax[..., None])
    row_total = jnp.sum(expw, axis=-1)
    acc_sum = jnp.einsum(
        "kgqp,pkd->kgqd",
        expw.astype(jnp.bfloat16),
        values_three,
        preferred_element_type=jnp.float32,
    )
    attn_out = (acc_sum / row_total[..., None]).astype(jnp.bfloat16)
    log_total = rowmax + jnp.log(row_total)
    delta = jnp.einsum("qkgd,kgqd->kgq", grad_four, attn_out, preferred_element_type=jnp.float32)

    probs = jnp.exp(scores - log_total[..., None])
    value_part = jnp.einsum(
        "kgqp,qkgd->pkd", probs.astype(jnp.bfloat16), grad_four, preferred_element_type=jnp.float32
    )
    grad_probs = jnp.einsum(
        "qkgd,pkd->kgqp", grad_four, values_three, preferred_element_type=jnp.float32
    )
    grad_scores = (probs * (grad_probs - delta[..., None])).astype(jnp.bfloat16)
    query_part = (
        jnp.einsum("kgqp,pkd->qkgd", grad_scores, keys_three, preferred_element_type=jnp.float32)
        * soft_scale
    )
    key_part = (
        jnp.einsum("kgqp,qkgd->pkd", grad_scores, query_four, preferred_element_type=jnp.float32)
        * soft_scale
    )
    grad_query = query_part.reshape(tok_rows, heads_kv * group_size * HD).astype(jnp.bfloat16)

    partial_kv = jnp.concatenate(
        [key_part.reshape(window, kv_cols), value_part.reshape(window, kv_cols)], axis=1
    )
    span = half * tok_rows
    from_other = lax.ppermute(partial_kv[span : 2 * span].astype(jnp.bfloat16), "ctx", sibling)
    back_stack = jnp.concatenate([partial_kv[2 * span :], partial_kv[:span]], axis=0)
    back_stack = lax.dynamic_update_slice_in_dim(
        back_stack,
        lax.dynamic_slice_in_dim(back_stack, parity * tok_rows, span, 0)
        + from_other.astype(jnp.float32),
        parity * tok_rows,
        0,
    )
    total_kv = back_stack[:tok_rows]
    for i in reversed(range(half)):
        piece = back_stack[(i + 1) * tok_rows : (i + 2) * tok_rows].astype(jnp.bfloat16)
        total_kv = total_kv + shifted(piece, "ctx", -2 * (i + 1)).astype(jnp.float32)
    grad_key = total_kv[:, :kv_cols].astype(jnp.bfloat16)
    grad_value = total_kv[:, kv_cols:].astype(jnp.bfloat16)
    own_grads = jnp.concatenate([grad_key, grad_value], axis=1)
    both_rows, own_grads = lax.optimization_barrier((both_rows, own_grads))
    every_grads = lax.all_to_all(
        jnp.broadcast_to(own_grads[None], (tp_size,) + own_grads.shape), "tp", 0, 0, tiled=True
    )
    grad_input = jnp.einsum(
        "jrkc,jkdc->rd",
        every_grads.reshape(tp_size, tok_rows, 2, kv_cols),
        both_rows,
        preferred_element_type=jnp.float32,
    ).astype(jnp.bfloat16)
    return (grad_query, grad_key, grad_value, grad_input)


def solution(mesh):
    in_specs = (
        P("ctx", "tp"),
        P("ctx", "tp"),
        P("ctx", "tp"),
        P("ctx", "tp"),
        P(None, "tp"),
        P(None, "tp"),
        P("ctx"),
    )
    out_specs = (P("ctx", "tp"), P("ctx", "tp"), P("ctx", "tp"), P("ctx", "tp"))
    return jax.shard_map(shards, mesh=mesh, in_specs=in_specs, out_specs=out_specs, check_vma=False)
```
